1024 devices in a mesh: fsdp: 32 (over z), ty: 4 (over y_lo, core), tx: 8 (over y_hi, x).
Axes of the slice: x: 4, y: 4 (y_hi: 2, y_lo: 2; y = y_hi * 2 + y_lo), z: 32, core: 2. Of those that a mesh axis runs over, the one named last changes fastest.
Arguments:
- q_raw: bfloat16 [64, 32, 64, 1536], P('fsdp', 'ty', 'tx'), may hold values from -6 to 6
- k_raw: bfloat16 [64, 32, 64, 1536], P('fsdp', 'ty', 'tx'), may hold values from -6 to 6
- values: bfloat16 [64, 32, 64, 1536], P('fsdp', 'ty', 'tx'), may hold values from -6 to 6
- d_out: bfloat16 [64, 32, 64, 1536], P('fsdp', 'ty', 'tx'), may hold values from -6 to 6
- q_gain: float32 [128], P('fsdp'), may hold values from 0.1 to 1.9
- k_gain: float32 [128], P('fsdp'), may hold values from 0.1 to 1.9
- windows: int32 [12, 2], replicated, may hold values from 1 to 3, as said below
Outputs:
- out: bfloat16 [64, 32, 64, 1536], P('fsdp', 'ty', 'tx')
- q_grad: bfloat16 [64, 32, 64, 1536], P('fsdp', 'ty', 'tx')
- k_grad: bfloat16 [64, 32, 64, 1536], P('fsdp', 'ty', 'tx')
- v_grad: bfloat16 [64, 32, 64, 1536], P('fsdp', 'ty', 'tx')
- q_gain_grad: float32 [128], P('fsdp')
- k_gain_grad: float32 [128], P('fsdp')
The draws below stay inside these ranges and needn't reach their ends.
Inputs may be any that keep to these rules, and one draw needn't show every extreme that they name: `windows`: every entry is 1 or 3; in each of the two columns some head has 3.
All inputs are finite; a program needn't handle non-finite values.
Results may differ from the reference program's by a relative error of at most 0.0083.
Values may be sent and summed in bfloat16 or wider, within the bound.
No kernel may reach another device: no remote copies, remote signals or barrier semaphores. Data moves between devices by JAX's collectives and lax.ppermute only.
A program may use at most 64 MiB of HBM per device.

```python
import math
import jax
import jax.numpy as jnp
from jax import lax

HEADS = 12
HEAD_DIM = 128
TILE = 8
FRAMES = 64
HEIGHT = 32
WIDTH = 64


def draw_windows(key, part):
    reach_base = jax.random.randint(jax.random.fold_in(key, 11), (HEADS, 2), 0, 2)
    chosen = jax.random.randint(jax.random.fold_in(key, 12), (2,), 0, HEADS)
    forced = (jnp.arange(HEADS)[:, None] == chosen[None, :]).astype(jnp.int32)
    return (2 * jnp.maximum(reach_base, forced) + 1).astype(jnp.int32)


def level_of(own_key, dims, cuts, smallest, largest):
    def one(dim, parts):
        draws = jax.random.uniform(jax.random.fold_in(jax.random.fold_in(own_key, 6), dim), (parts,), jnp.float32, smallest / len(cuts), largest / len(cuts))
        return jnp.repeat(jnp.exp(draws), dims[dim] // parts).reshape((-1,) + (1,) * (len(dims) - dim - 1))

    gain = one(*cuts[0])
    for cut in cuts[1:]:
        gain = gain * one(*cut)
    return gain


def noise(rng, shape, scale, reach, cuts=(), kind=jnp.bfloat16):
    values = scale * jax.random.normal(rng, shape, jnp.float32)
    if cuts:
        values = values * level_of(rng, shape, cuts, -0.22, 0.18)
    return jnp.clip(values, -reach, reach).astype(kind)


def setup_inputs(seed: int = 0) -> dict:
    key_of = jax.random.split(jax.random.key(seed), 8)
    q_raw = noise(key_of[0], (FRAMES, HEIGHT, WIDTH, HEADS * HEAD_DIM), 1.0, 6.0, ((0, 32), (1, 4), (2, 8)))
    k_raw = noise(key_of[1], (FRAMES, HEIGHT, WIDTH, HEADS * HEAD_DIM), 1.0, 6.0, ((0, 32), (1, 4), (2, 8)))
    values = noise(key_of[2], (FRAMES, HEIGHT, WIDTH, HEADS * HEAD_DIM), 1.0, 6.0, ((0, 32), (1, 4), (2, 8)))
    d_out = noise(key_of[3], (FRAMES, HEIGHT, WIDTH, HEADS * HEAD_DIM), 1.0, 6.0, ((0, 32), (1, 4), (2, 8)))
    q_gain = jnp.clip(1.0 + 0.18 * jax.random.normal(key_of[4], (HEAD_DIM,), jnp.float32), 0.1, 1.9)
    k_gain = jnp.clip(1.0 + 0.18 * jax.random.normal(key_of[5], (HEAD_DIM,), jnp.float32), 0.1, 1.9)
    windows = draw_windows(jax.random.fold_in(key_of[7], 71), 0)
    return {"q_raw": q_raw, "k_raw": k_raw, "values": values, "d_out": d_out, "q_gain": q_gain, "k_gain": k_gain, "windows": windows}


NORM_EPS = 1e-06
NEIGHBOUR_STEPS = [(row_step, col_step) for row_step in (-1, 0, 1) for col_step in (-1, 0, 1)]

def product(form, left, right):
    return jnp.einsum(form, left.astype(jnp.float32), right.astype(jnp.float32), precision=lax.Precision.HIGHEST)

def to_tiles(field_grid, tile_size):
    row_count, col_count, feature_count = field_grid.shape
    shaped = field_grid.reshape(row_count // tile_size, tile_size, col_count // tile_size, tile_size, feature_count)
    return shaped.transpose(0, 2, 1, 3, 4).reshape(row_count // tile_size, col_count // tile_size, tile_size * tile_size, feature_count)

def from_tiles(tile_view, tile_size):
    tile_rows, tile_cols, cell_count, feature_count = tile_view.shape
    shaped = tile_view.reshape(tile_rows, tile_cols, tile_size, tile_size, feature_count).transpose(0, 2, 1, 3, 4)
    return shaped.reshape(tile_rows * tile_size, tile_cols * tile_size, feature_count)

def neighbours(padded):
    tile_rows = padded.shape[0] - 2
    tile_cols = padded.shape[1] - 2
    shifted_views = [padded[1 + row_step:1 + row_step + tile_rows, 1 + col_step:1 + col_step + tile_cols] for row_step, col_step in NEIGHBOUR_STEPS]
    return jnp.stack(shifted_views, axis=2)

def window_live(first_row, first_col, tile_rows, tile_cols, total_rows, total_cols, windows):
    reach_rows = (windows[:, 0] - 1) // 2
    reach_cols = (windows[:, 1] - 1) // 2
    row_index = first_row + jnp.arange(tile_rows, dtype=jnp.int32)
    col_index = first_col + jnp.arange(tile_cols, dtype=jnp.int32)
    pieces = []
    for row_step, col_step in NEIGHBOUR_STEPS:
        inside_rows = ((row_index + row_step >= 0) & (row_index + row_step < total_rows))[:, None, None]
        inside_cols = ((col_index + col_step >= 0) & (col_index + col_step < total_cols))[None, :, None]
        within = ((abs(row_step) <= reach_rows) & (abs(col_step) <= reach_cols))[None, None, :]
        pieces.append(inside_rows & inside_cols & within)
    return jnp.stack(pieces, axis=-1)

def normalize(raw_field, norm_gain, head_count):
    floats = raw_field.astype(jnp.float32)
    floats = floats.reshape(floats.shape[:-1] + (head_count, norm_gain.shape[0]))
    inverse = lax.rsqrt(lax.optimization_barrier(jnp.mean(floats * floats, axis=-1, keepdims=True)) + NORM_EPS)
    normed = floats * inverse
    return (normed, inverse, (normed * norm_gain).astype(jnp.bfloat16))

def norm_backward(upstream, normed, inverse, norm_gain):
    gain_part = lax.optimization_barrier(jnp.sum(upstream * normed, axis=tuple(range(upstream.ndim - 1))))
    scaled = upstream * norm_gain
    raw_grad = inverse * (scaled - normed * lax.optimization_barrier(jnp.mean(scaled * normed, axis=-1, keepdims=True)))
    return (raw_grad, gain_part)

def query_side(queries, keys_near, values_near, grad_out, window_open, score_scale):
    scores = product('yxqhc,yxnkhc->yxhqnk', queries, keys_near) * score_scale
    open_mask = window_open[:, :, :, None, :, None]
    weights = jnp.where(open_mask, jnp.exp(scores), 0.0)
    totals = lax.optimization_barrier(jnp.sum(weights, axis=(4, 5)))
    shares = weights / totals[..., None, None]
    shares_low = shares.astype(jnp.bfloat16)
    output = product('yxhqnk,yxnkhc->yxqhc', shares_low, values_near).astype(jnp.bfloat16)
    output_back = lax.optimization_barrier(output).astype(jnp.float32)
    row_delta = lax.optimization_barrier(jnp.sum(grad_out.astype(jnp.float32) * output_back, axis=-1))
    share_grad = product('yxqhc,yxnkhc->yxhqnk', grad_out, values_near)
    score_grad = (shares * (share_grad - jnp.swapaxes(row_delta, 2, 3)[..., None, None])).astype(jnp.bfloat16)
    query_grad = product('yxhqnk,yxnkhc->yxqhc', score_grad, keys_near) * score_scale
    return (output, jnp.swapaxes(totals, 2, 3), row_delta, query_grad)

def key_side(keys, value_tiles, queries_near, grads_near, totals_near, delta_near, window_open, score_scale):
    scores = product('yxnqhc,yxkhc->yxhnqk', queries_near, keys) * score_scale
    open_mask = window_open[:, :, :, :, None, None]
    weights = jnp.where(open_mask, jnp.exp(scores), 0.0)
    divisor = jnp.where(open_mask, jnp.moveaxis(totals_near, 4, 2)[..., None], 1.0)
    shares = weights / divisor
    shares_low = shares.astype(jnp.bfloat16)
    value_grad = product('yxhnqk,yxnqhc->yxkhc', shares_low, grads_near)
    share_grad = product('yxnqhc,yxkhc->yxhnqk', grads_near, value_tiles)
    score_grad = (shares * (share_grad - jnp.moveaxis(delta_near, 4, 2)[..., None])).astype(jnp.bfloat16)
    key_grad = product('yxhnqk,yxnqhc->yxkhc', score_grad, queries_near) * score_scale
    return (key_grad, value_grad)

def tiled(field_grid, head_count):
    tile_view = to_tiles(field_grid, TILE)
    return tile_view.reshape(tile_view.shape[:3] + (head_count, -1))

def to_field(tile_view):
    flat_view = tile_view.reshape(tile_view.shape[:3] + (-1,))
    return from_tiles(flat_view, TILE)

def padded_near(tile_view):
    pad_widths = ((1, 1), (1, 1)) + ((0, 0),) * (tile_view.ndim - 2)
    return neighbours(jnp.pad(tile_view, pad_widths))

def one_video(q_raw, k_raw, values, d_out, q_gain, k_gain, windows):
    row_count, col_count, feature_count = q_raw.shape
    score_scale = 1.0 / math.sqrt(HEAD_DIM)
    q_normed, q_inverse, q_hat = normalize(q_raw, q_gain, HEADS)
    k_normed, k_inverse, k_hat = normalize(k_raw, k_gain, HEADS)
    queries = tiled(q_hat.reshape(row_count, col_count, feature_count), HEADS)
    keys = tiled(k_hat.reshape(row_count, col_count, feature_count), HEADS)
    value_tiles = tiled(values, HEADS)
    grad_tiles = tiled(d_out, HEADS)
    tile_rows = row_count // TILE
    tile_cols = col_count // TILE
    window_open = window_live(0, 0, tile_rows, tile_cols, tile_rows, tile_cols, windows)
    keys_near = padded_near(keys)
    values_near = padded_near(value_tiles)

    def query_row(row_items):
        lifted = [item[None] for item in row_items]
        results = query_side(lifted[0], lifted[1], lifted[2], lifted[3], lifted[4], score_scale)
        return tuple((result[0] for result in results))
    output, totals, row_delta, query_grad = lax.map(query_row, (queries, keys_near, values_near, grad_tiles, window_open))
    queries_near = padded_near(queries)
    grads_near = padded_near(grad_tiles)
    totals_near = padded_near(totals)
    delta_near = padded_near(row_delta)

    def key_row(row_items):
        lifted = [item[None] for item in row_items]
        results = key_side(lifted[0], lifted[1], lifted[2], lifted[3], lifted[4], lifted[5], lifted[6], score_scale)
        return tuple((result[0] for result in results))
    key_grad, value_grad = lax.map(key_row, (keys, value_tiles, queries_near, grads_near, totals_near, delta_near, window_open))
    q_upstream = to_field(query_grad).reshape(q_normed.shape)
    k_upstream = to_field(key_grad).reshape(k_normed.shape)
    q_field_grad, q_part = norm_backward(q_upstream, q_normed, q_inverse, q_gain)
    k_field_grad, k_part = norm_backward(k_upstream, k_normed, k_inverse, k_gain)
    return (to_field(output), q_field_grad.reshape(row_count, col_count, feature_count).astype(jnp.bfloat16), k_field_grad.reshape(row_count, col_count, feature_count).astype(jnp.bfloat16), to_field(value_grad).astype(jnp.bfloat16), q_part, k_part)

def reference(q_raw, k_raw, values, d_out, q_gain, k_gain, windows):

    def video_step(video_items):
        return one_video(video_items[0], video_items[1], video_items[2], video_items[3], q_gain, k_gain, windows)
    output, q_grad, k_grad, v_grad, q_part, k_part = lax.map(video_step, (q_raw, k_raw, values, d_out))
    return (output, q_grad, k_grad, v_grad, lax.optimization_barrier(jnp.sum(q_part, axis=0)), lax.optimization_barrier(jnp.sum(k_part, axis=0)))
```

```python
import math

import jax
import jax.numpy as jnp
from jax import lax
from jax.sharding import PartitionSpec as P

TILE = 8


NORM_EPS = 1e-06


def padded(cells, sides, width):
    for axis, dim in sides:
        count = lax.axis_size(axis)
        ends = count - 1
        head = lax.slice_in_dim(cells, 0, width, axis=dim)
        tail = lax.slice_in_dim(cells, cells.shape[dim] - width, cells.shape[dim], axis=dim)
        cells = jnp.concatenate(
            [
                lax.ppermute(tail, axis, [(i, (i + 1) % count) for i in range(ends)]),
                cells,
                lax.ppermute(head, axis, [((i + 1) % count, i) for i in range(ends)]),
            ],
            axis=dim,
        )
    return cells


def xor_sum(cells, axis):
    count = lax.axis_size(axis)
    step = 1
    while step < count:
        cells = cells + lax.ppermute(cells, axis, [(i, i ^ step) for i in range(count)])
        step *= 2
    return cells


def product(form, left, right):
    return jnp.einsum(form, left, right, preferred_element_type=jnp.float32)


def normalize(raw_field, norm_gain, head_count):
    floats = raw_field.astype(jnp.float32)
    floats = floats.reshape(floats.shape[:-1] + (head_count, norm_gain.shape[0]))
    inverse = lax.rsqrt(jnp.mean(floats * floats, axis=-1, keepdims=True) + NORM_EPS)
    normed = floats * inverse
    return (normed, inverse, (normed * norm_gain).astype(jnp.bfloat16))


def norm_backward(upstream, normed, inverse, norm_gain):
    gain_part = jnp.sum(upstream * normed, axis=tuple(range(upstream.ndim - 1)))
    scaled = upstream * norm_gain
    raw_grad = inverse * (scaled - normed * jnp.mean(scaled * normed, axis=-1, keepdims=True))
    return (raw_grad, gain_part)


def open_pairs(windows, tile_size):
    span = 3 * tile_size
    spots = jnp.arange(span * span, dtype=jnp.int32)
    step_rows = spots // span // tile_size - 1
    step_cols = spots % span // tile_size - 1
    tile_row = lax.axis_index("ty") + step_rows
    tile_col = lax.axis_index("tx") + step_cols
    inside = (
        (tile_row >= 0)
        & (tile_row < lax.axis_size("ty"))
        & (tile_col >= 0)
        & (tile_col < lax.axis_size("tx"))
    )
    reach_rows = ((windows[:, 0] - 1) // 2)[:, None]
    reach_cols = ((windows[:, 1] - 1) // 2)[:, None]
    within = (jnp.abs(step_rows)[None, :] <= reach_rows) & (
        jnp.abs(step_cols)[None, :] <= reach_cols
    )
    return inside[None, :] & within


def query_side(queries, keys_near, values_near, grad_out, open_mask, score_scale):
    scores = product("qhc,mhc->hqm", queries, keys_near) * score_scale
    weights = jnp.where(open_mask[:, None, :], jnp.exp(scores), 0.0)
    totals = jnp.sum(weights, axis=2)
    shares = weights / totals[:, :, None]
    shares_low = shares.astype(jnp.bfloat16)
    output = product("hqm,mhc->qhc", shares_low, values_near).astype(jnp.bfloat16)
    output_back = lax.optimization_barrier(output).astype(jnp.float32)
    row_delta = jnp.sum(grad_out.astype(jnp.float32) * output_back, axis=-1)
    share_grad = product("qhc,mhc->hqm", grad_out, values_near)
    score_grad = (shares * (share_grad - row_delta.T[:, :, None])).astype(jnp.bfloat16)
    query_grad = product("hqm,mhc->qhc", score_grad, keys_near) * score_scale
    return (output, totals.T, row_delta, query_grad)


def key_side(
    keys, value_rows, queries_near, grads_near, totals_near, delta_near, open_mask, score_scale
):
    scores = product("khc,mhc->hkm", keys, queries_near) * score_scale
    mask_rows = open_mask[:, None, :]
    weights = jnp.where(mask_rows, jnp.exp(scores), 0.0)
    divisor = jnp.where(open_mask, totals_near.T, 1.0)[:, None, :]
    shares = weights / divisor
    shares_low = shares.astype(jnp.bfloat16)
    value_grad = product("hkm,mhc->khc", shares_low, grads_near)
    share_grad = product("mhc,khc->hkm", grads_near, value_rows)
    score_grad = (shares * (share_grad - delta_near.T[:, None, :])).astype(jnp.bfloat16)
    key_grad = product("hkm,mhc->khc", score_grad, queries_near) * score_scale
    return (key_grad, value_grad)


def body(q_raw, k_raw, values, d_out, q_gain, k_gain, windows):
    head_count = windows.shape[0]
    share_len = q_gain.shape[0]
    head_size = share_len * lax.axis_size("fsdp")
    gain_slots = jnp.zeros((2, head_size), jnp.float32)
    gain_slots = lax.dynamic_update_slice_in_dim(
        gain_slots, jnp.stack([q_gain, k_gain]), lax.axis_index("fsdp") * share_len, 1
    )
    gains = xor_sum(gain_slots, "fsdp")
    q_gain_all, k_gain_all = gains[0], gains[1]
    frame_count, row_count, col_count, feature_count = q_raw.shape
    score_scale = 1.0 / math.sqrt(head_size)
    sides = (("ty", 2), ("tx", 3))
    arrived = padded(jnp.stack([k_raw, values]), sides, TILE)
    arrived_back = padded(jnp.stack([q_raw, d_out]), sides, TILE)
    q_normed, q_inverse, q_hat = normalize(q_raw, q_gain_all, head_count)
    k_normed, k_inverse, k_hat = normalize(k_raw, k_gain_all, head_count)
    k_hat_near = normalize(arrived[0], k_gain_all, head_count)[2]
    q_hat_near = normalize(arrived_back[0], q_gain_all, head_count)[2]
    q_flat = q_hat.reshape(q_raw.shape)
    k_flat = k_hat.reshape(k_raw.shape)
    open_mask = open_pairs(windows, TILE)
    local_rows = row_count * col_count
    near_rows = (row_count + 2 * TILE) * (col_count + 2 * TILE)

    def as_local(field):
        return field.reshape(frame_count, local_rows, head_count, head_size)

    def as_near(field):
        return field.reshape(frame_count, near_rows, head_count, head_size)

    def frame_query(queries, keys_near, values_near, grad_out):
        return query_side(queries, keys_near, values_near, grad_out, open_mask, score_scale)

    output, totals, row_delta, query_grad = jax.vmap(frame_query)(
        as_local(q_flat), as_near(k_hat_near), as_near(arrived[1]), as_local(d_out)
    )
    stat_grid = jnp.stack([totals, row_delta]).reshape(
        2, frame_count, row_count, col_count, head_count
    )
    row_sums = padded(stat_grid, (("ty", 2), ("tx", 3)), TILE)
    row_sums = row_sums.reshape(2, frame_count, near_rows, head_count)
    query_fields = q_hat_near
    grad_fields = arrived_back[1]

    def frame_key(keys, value_rows, queries_near, grads_near, totals_near, delta_near):
        return key_side(
            keys,
            value_rows,
            queries_near,
            grads_near,
            totals_near,
            delta_near,
            open_mask,
            score_scale,
        )

    key_grad, value_grad = jax.vmap(frame_key)(
        as_local(k_flat),
        as_local(values),
        as_near(query_fields),
        as_near(grad_fields),
        row_sums[0],
        row_sums[1],
    )
    q_upstream = query_grad.reshape(q_normed.shape)
    k_upstream = key_grad.reshape(k_normed.shape)
    q_field_grad, q_part = norm_backward(q_upstream, q_normed, q_inverse, q_gain_all)
    k_field_grad, k_part = norm_backward(k_upstream, k_normed, k_inverse, k_gain_all)
    gain_parts = jnp.stack([q_part, k_part])
    plane_sum = xor_sum(xor_sum(gain_parts, "tx"), "ty")
    owner_count = lax.axis_size("fsdp")
    pieces = plane_sum.reshape(2, owner_count, share_len).transpose(1, 0, 2)
    owned = lax.all_to_all(pieces, "fsdp", 0, 0, tiled=True).sum(axis=0)
    return (
        output.reshape(q_raw.shape),
        q_field_grad.reshape(q_raw.shape).astype(jnp.bfloat16),
        k_field_grad.reshape(k_raw.shape).astype(jnp.bfloat16),
        value_grad.reshape(values.shape).astype(jnp.bfloat16),
        owned[0],
        owned[1],
    )


def solution(mesh):
    return jax.shard_map(
        body,
        mesh=mesh,
        in_specs=(
            P("fsdp", "ty", "tx", None),
            P("fsdp", "ty", "tx", None),
            P("fsdp", "ty", "tx", None),
            P("fsdp", "ty", "tx", None),
            P("fsdp"),
            P("fsdp"),
            P(),
        ),
        out_specs=(
            P("fsdp", "ty", "tx", None),
            P("fsdp", "ty", "tx", None),
            P("fsdp", "ty", "tx", None),
            P("fsdp", "ty", "tx", None),
            P("fsdp"),
            P("fsdp"),
        ),
        check_vma=False,
    )
```

```python
import math

import jax
import jax.numpy as jnp
from jax import lax
from jax.sharding import PartitionSpec as P

TILE = 8


NORM_EPS = 1e-06


def padded(cells, sides, width):
    for axis, dim in sides:
        count = lax.axis_size(axis)
        ends = count - 1
        head = lax.slice_in_dim(cells, 0, width, axis=dim)
        tail = lax.slice_in_dim(cells, cells.shape[dim] - width, cells.shape[dim], axis=dim)
        cells = jnp.concatenate(
            [
                lax.ppermute(tail, axis, [(i, (i + 1) % count) for i in range(ends)]),
                cells,
                lax.ppermute(head, axis, [((i + 1) % count, i) for i in range(ends)]),
            ],
            axis=dim,
        )
    return cells


def xor_sum(cells, axis):
    count = lax.axis_size(axis)
    step = 1
    while step < count:
        cells = cells + lax.ppermute(cells, axis, [(i, i ^ step) for i in range(count)])
        step *= 2
    return cells


def product(form, left, right):
    return jnp.einsum(form, left, right, preferred_element_type=jnp.float32)


def normalize(raw_field, norm_gain, head_count):
    floats = raw_field.astype(jnp.float32)
    floats = floats.reshape(floats.shape[:-1] + (head_count, norm_gain.shape[0]))
    inverse = lax.rsqrt(jnp.mean(floats * floats, axis=-1, keepdims=True) + NORM_EPS)
    normed = floats * inverse
    return (normed, inverse, (normed * norm_gain).astype(jnp.bfloat16))


def norm_backward(upstream, normed, inverse, norm_gain):
    gain_part = jnp.sum(upstream * normed, axis=tuple(range(upstream.ndim - 1)))
    scaled = upstream * norm_gain
    raw_grad = inverse * (scaled - normed * jnp.mean(scaled * normed, axis=-1, keepdims=True))
    return (raw_grad, gain_part)


def open_pairs(windows, tile_size):
    span = 3 * tile_size
    spots = jnp.arange(span * span, dtype=jnp.int32)
    step_rows = spots // span // tile_size - 1
    step_cols = spots % span // tile_size - 1
    tile_row = lax.axis_index("ty") + step_rows
    tile_col = lax.axis_index("tx") + step_cols
    inside = (
        (tile_row >= 0)
        & (tile_row < lax.axis_size("ty"))
        & (tile_col >= 0)
        & (tile_col < lax.axis_size("tx"))
    )
    reach_rows = ((windows[:, 0] - 1) // 2)[:, None]
    reach_cols = ((windows[:, 1] - 1) // 2)[:, None]
    within = (jnp.abs(step_rows)[None, :] <= reach_rows) & (
        jnp.abs(step_cols)[None, :] <= reach_cols
    )
    return inside[None, :] & within


def gathered(cells, sides, width):
    for axis, dim in reversed(sides):
        count = lax.axis_size(axis)
        ends = count - 1
        full = cells.shape[dim]
        head = lax.slice_in_dim(cells, 0, width, axis=dim)
        middle = lax.slice_in_dim(cells, width, full - width, axis=dim).astype(jnp.float32)
        tail = lax.slice_in_dim(cells, full - width, full, axis=dim)
        from_right = lax.ppermute(head.astype(jnp.bfloat16), axis, [((i + 1) % count, i) for i in range(ends)])
        from_left = lax.ppermute(tail.astype(jnp.bfloat16), axis, [(i, (i + 1) % count) for i in range(ends)])
        cells = middle + from_right.astype(jnp.float32) + from_left.astype(jnp.float32)
    return cells


def raw_backward(upstream, normed, inverse, norm_gain):
    scaled = upstream * norm_gain
    return inverse * (scaled - normed * jnp.mean(scaled * normed, axis=-1, keepdims=True))


def query_side(queries, keys_near, values_near, grad_out, open_mask, score_scale):
    scores = product("qhc,mhc->hqm", queries, keys_near) * score_scale
    weights = jnp.where(open_mask[:, None, :], jnp.exp(scores), 0.0)
    totals = jnp.sum(weights, axis=2)
    shares = weights / totals[:, :, None]
    shares_low = shares.astype(jnp.bfloat16)
    output = product("hqm,mhc->qhc", shares_low, values_near).astype(jnp.bfloat16)
    output_back = lax.optimization_barrier(output).astype(jnp.float32)
    row_delta = jnp.sum(grad_out.astype(jnp.float32) * output_back, axis=-1)
    share_grad = product("qhc,mhc->hqm", grad_out, values_near)
    score_grad = (shares * (share_grad - row_delta.T[:, :, None])).astype(jnp.bfloat16)
    query_grad = product("hqm,mhc->qhc", score_grad, keys_near) * score_scale
    value_part = product("hqm,qhc->mhc", shares_low, grad_out)
    key_part = product("hqm,qhc->mhc", score_grad, queries) * score_scale
    return (output, query_grad, key_part, value_part)


def body(q_raw, k_raw, values, d_out, q_gain, k_gain, windows):
    head_count = windows.shape[0]
    share_len = q_gain.shape[0]
    head_size = share_len * lax.axis_size("fsdp")
    gain_slots = jnp.zeros((2, head_size), jnp.float32)
    gain_slots = lax.dynamic_update_slice_in_dim(
        gain_slots, jnp.stack([q_gain, k_gain]), lax.axis_index("fsdp") * share_len, 1
    )
    gains = xor_sum(gain_slots, "fsdp")
    q_gain_all, k_gain_all = gains[0], gains[1]
    frame_count, row_count, col_count, feature_count = q_raw.shape
    score_scale = 1.0 / math.sqrt(head_size)
    sides = (("ty", 2), ("tx", 3))
    arrived = padded(jnp.stack([k_raw, values]), sides, TILE)
    q_normed, q_inverse, q_hat = normalize(q_raw, q_gain_all, head_count)
    k_normed, k_inverse, _ = normalize(k_raw, k_gain_all, head_count)
    k_normed_near, _, k_hat_near = normalize(arrived[0], k_gain_all, head_count)
    open_mask = open_pairs(windows, TILE)
    local_rows = row_count * col_count
    near_rows = (row_count + 2 * TILE) * (col_count + 2 * TILE)

    def as_local(field):
        return field.reshape(frame_count, local_rows, head_count, head_size)

    def as_near(field):
        return field.reshape(frame_count, near_rows, head_count, head_size)

    def frame_query(queries, keys_near, values_near, grad_out):
        return query_side(queries, keys_near, values_near, grad_out, open_mask, score_scale)

    output, query_grad, key_part, value_part = jax.vmap(frame_query)(
        as_local(q_hat), as_near(k_hat_near), as_near(arrived[1]), as_local(d_out)
    )
    q_upstream = query_grad.reshape(q_normed.shape)
    q_part = jnp.sum(q_upstream * q_normed, axis=(0, 1, 2, 3))
    k_part = jnp.sum(key_part * as_near(k_normed_near), axis=(0, 1, 2))
    gain_parts = jnp.stack([q_part, k_part])
    plane_sum = xor_sum(xor_sum(gain_parts, "tx"), "ty")
    owner_count = lax.axis_size("fsdp")
    pieces = plane_sum.reshape(2, owner_count, share_len).transpose(1, 0, 2)
    owned = lax.all_to_all(pieces, "fsdp", 0, 0, tiled=True).sum(axis=0)
    near_shape = (2, frame_count, row_count + 2 * TILE, col_count + 2 * TILE, feature_count)
    parts = jnp.stack([key_part, value_part]).reshape(near_shape)
    summed = gathered(parts, sides, TILE)
    k_upstream = summed[0].reshape(k_normed.shape)
    q_field_grad = raw_backward(q_upstream, q_normed, q_inverse, q_gain_all)
    k_field_grad = raw_backward(k_upstream, k_normed, k_inverse, k_gain_all)
    return (
        output.reshape(q_raw.shape),
        q_field_grad.reshape(q_raw.shape).astype(jnp.bfloat16),
        k_field_grad.reshape(k_raw.shape).astype(jnp.bfloat16),
        summed[1].astype(jnp.bfloat16),
        owned[0],
        owned[1],
    )


def solution(mesh):
    return jax.shard_map(
        body,
        mesh=mesh,
        in_specs=(
            P("fsdp", "ty", "tx", None),
            P("fsdp", "ty", "tx", None),
            P("fsdp", "ty", "tx", None),
            P("fsdp", "ty", "tx", None),
            P("fsdp"),
            P("fsdp"),
            P(),
        ),
        out_specs=(
            P("fsdp", "ty", "tx", None),
            P("fsdp", "ty", "tx", None),
            P("fsdp", "ty", "tx", None),
            P("fsdp", "ty", "tx", None),
            P("fsdp"),
            P("fsdp"),
        ),
        check_vma=False,
    )
```

```python
import math

import jax
import jax.numpy as jnp
from jax import lax
from jax.sharding import PartitionSpec as P

TILE = 8


NORM_EPS = 1e-06


def padded(cells, sides, width):
    for axis, dim in sides:
        count = lax.axis_size(axis)
        ends = count - 1
        head = lax.slice_in_dim(cells, 0, width, axis=dim)
        tail = lax.slice_in_dim(cells, cells.shape[dim] - width, cells.shape[dim], axis=dim)
        cells = jnp.concatenate(
            [
                lax.ppermute(tail, axis, [(i, (i + 1) % count) for i in range(ends)]),
                cells,
                lax.ppermute(head, axis, [((i + 1) % count, i) for i in range(ends)]),
            ],
            axis=dim,
        )
    return cells


def xor_sum(cells, axis):
    count = lax.axis_size(axis)
    step = 1
    while step < count:
        cells = cells + lax.ppermute(cells, axis, [(i, i ^ step) for i in range(count)])
        step *= 2
    return cells


def product(form, left, right):
    return jnp.einsum(form, left, right, preferred_element_type=jnp.float32)


def normalize(raw_field, norm_gain, head_count):
    floats = raw_field.astype(jnp.float32)
    floats = floats.reshape(floats.shape[:-1] + (head_count, norm_gain.shape[0]))
    inverse = lax.rsqrt(jnp.mean(floats * floats, axis=-1, keepdims=True) + NORM_EPS)
    normed = floats * inverse
    return (normed, inverse, (normed * norm_gain).astype(jnp.bfloat16))


def norm_backward(upstream, normed, inverse, norm_gain):
    gain_part = jnp.sum(upstream * normed, axis=tuple(range(upstream.ndim - 1)))
    scaled = upstream * norm_gain
    raw_grad = inverse * (scaled - normed * jnp.mean(scaled * normed, axis=-1, keepdims=True))
    return (raw_grad, gain_part)


def open_pairs(windows, tile_size):
    span = 3 * tile_size
    spots = jnp.arange(span * span, dtype=jnp.int32)
    step_rows = spots // span // tile_size - 1
    step_cols = spots % span // tile_size - 1
    tile_row = lax.axis_index("ty") + step_rows
    tile_col = lax.axis_index("tx") + step_cols
    inside = (
        (tile_row >= 0)
        & (tile_row < lax.axis_size("ty"))
        & (tile_col >= 0)
        & (tile_col < lax.axis_size("tx"))
    )
    reach_rows = ((windows[:, 0] - 1) // 2)[:, None]
    reach_cols = ((windows[:, 1] - 1) // 2)[:, None]
    within = (jnp.abs(step_rows)[None, :] <= reach_rows) & (
        jnp.abs(step_cols)[None, :] <= reach_cols
    )
    return inside[None, :] & within


def gathered(cells, sides, width):
    for axis, dim in reversed(sides):
        count = lax.axis_size(axis)
        ends = count - 1
        full = cells.shape[dim]
        head = lax.slice_in_dim(cells, 0, width, axis=dim)
        middle = lax.slice_in_dim(cells, width, full - width, axis=dim).astype(jnp.float32)
        tail = lax.slice_in_dim(cells, full - width, full, axis=dim)
        from_right = lax.ppermute(head.astype(jnp.bfloat16), axis, [((i + 1) % count, i) for i in range(ends)])
        from_left = lax.ppermute(tail.astype(jnp.bfloat16), axis, [(i, (i + 1) % count) for i in range(ends)])
        cells = middle + from_right.astype(jnp.float32) + from_left.astype(jnp.float32)
    return cells


def raw_backward(upstream, normed, inverse, norm_gain):
    scaled = upstream * norm_gain
    return inverse * (scaled - normed * jnp.mean(scaled * normed, axis=-1, keepdims=True))


def query_side(queries, keys_near, values_near, grad_out, open_mask, score_scale):
    scores = product("qhc,mhc->hqm", queries, keys_near) * score_scale
    weights = jnp.where(open_mask[:, None, :], jnp.exp(scores), 0.0)
    totals = jnp.sum(weights, axis=2)
    shares = weights / totals[:, :, None]
    shares_low = shares.astype(jnp.bfloat16)
    output = product("hqm,mhc->qhc", shares_low, values_near).astype(jnp.bfloat16)
    output_back = lax.optimization_barrier(output).astype(jnp.float32)
    row_delta = jnp.sum(grad_out.astype(jnp.float32) * output_back, axis=-1)
    share_grad = product("qhc,mhc->hqm", grad_out, values_near)
    score_grad = (shares * (share_grad - row_delta.T[:, :, None])).astype(jnp.bfloat16)
    query_grad = product("hqm,mhc->qhc", score_grad, keys_near) * score_scale
    value_part = product("hqm,qhc->hmc", shares_low, grad_out)
    key_part = product("hqm,qhc->hmc", score_grad, queries) * score_scale
    return (output, query_grad, key_part, value_part)


def body(q_raw, k_raw, values, d_out, q_gain, k_gain, windows):
    head_count = windows.shape[0]
    share_len = q_gain.shape[0]
    head_size = share_len * lax.axis_size("fsdp")
    gain_slots = jnp.zeros((2, head_size), jnp.float32)
    gain_slots = lax.dynamic_update_slice_in_dim(
        gain_slots, jnp.stack([q_gain, k_gain]), lax.axis_index("fsdp") * share_len, 1
    )
    gains = xor_sum(gain_slots, "fsdp")
    q_gain_all, k_gain_all = gains[0], gains[1]
    frame_count, row_count, col_count, feature_count = q_raw.shape
    score_scale = 1.0 / math.sqrt(head_size)
    sides = (("ty", 2), ("tx", 3))
    arrived = padded(jnp.stack([k_raw, values]), sides, TILE)
    q_normed, q_inverse, q_hat = normalize(q_raw, q_gain_all, head_count)
    k_normed, k_inverse, _ = normalize(k_raw, k_gain_all, head_count)
    k_normed_near, _, k_hat_near = normalize(arrived[0], k_gain_all, head_count)
    open_mask = open_pairs(windows, TILE)
    local_rows = row_count * col_count
    near_rows = (row_count + 2 * TILE) * (col_count + 2 * TILE)

    def as_local(field):
        return field.reshape(frame_count, local_rows, head_count, head_size)

    def as_near(field):
        return field.reshape(frame_count, near_rows, head_count, head_size)

    def frame_query(queries, keys_near, values_near, grad_out):
        return query_side(queries, keys_near, values_near, grad_out, open_mask, score_scale)

    output, query_grad, key_part, value_part = jax.vmap(frame_query)(
        as_local(q_hat), as_near(k_hat_near), as_near(arrived[1]), as_local(d_out)
    )
    q_upstream = query_grad.reshape(q_normed.shape)
    q_part = jnp.sum(q_upstream * q_normed, axis=(0, 1, 2, 3))
    k_part = jnp.sum(key_part * jnp.swapaxes(as_near(k_normed_near), 1, 2), axis=(0, 1, 2))
    gain_parts = jnp.stack([q_part, k_part])
    plane_sum = xor_sum(xor_sum(gain_parts, "tx"), "ty")
    plane_sum, key_part, value_part = lax.optimization_barrier((plane_sum, key_part, value_part))
    owner_count = lax.axis_size("fsdp")
    pieces = plane_sum.reshape(2, owner_count, share_len).transpose(1, 0, 2)
    owned = lax.all_to_all(pieces, "fsdp", 0, 0, tiled=True).sum(axis=0)
    near_shape = (frame_count, head_count, row_count + 2 * TILE, col_count + 2 * TILE, head_size)

    def summed_of(part):
        cells = gathered(part.reshape(near_shape), sides, TILE)
        return cells.transpose(0, 2, 3, 1, 4)

    key_summed = summed_of(key_part)
    value_summed = summed_of(value_part)
    k_upstream = key_summed.reshape(k_normed.shape)
    q_field_grad = raw_backward(q_upstream, q_normed, q_inverse, q_gain_all)
    k_field_grad = raw_backward(k_upstream, k_normed, k_inverse, k_gain_all)
    return (
        output.reshape(q_raw.shape),
        q_field_grad.reshape(q_raw.shape).astype(jnp.bfloat16),
        k_field_grad.reshape(k_raw.shape).astype(jnp.bfloat16),
        value_summed.reshape(values.shape).astype(jnp.bfloat16),
        owned[0],
        owned[1],
    )


def solution(mesh):
    return jax.shard_map(
        body,
        mesh=mesh,
        in_specs=(
            P("fsdp", "ty", "tx", None),
            P("fsdp", "ty", "tx", None),
            P("fsdp", "ty", "tx", None),
            P("fsdp", "ty", "tx", None),
            P("fsdp"),
            P("fsdp"),
            P(),
        ),
        out_specs=(
            P("fsdp", "ty", "tx", None),
            P("fsdp", "ty", "tx", None),
            P("fsdp", "ty", "tx", None),
            P("fsdp", "ty", "tx", None),
            P("fsdp"),
            P("fsdp"),
        ),
        check_vma=False,
    )
```

```python
import math

import jax
import jax.numpy as jnp
from jax import lax
from jax.sharding import PartitionSpec as P

TILE = 8


NORM_EPS = 1e-06


def padded(cells, sides, width):
    for axis, dim in sides:
        count = lax.axis_size(axis)
        ends = count - 1
        head = lax.slice_in_dim(cells, 0, width, axis=dim)
        tail = lax.slice_in_dim(cells, cells.shape[dim] - width, cells.shape[dim], axis=dim)
        cells = jnp.concatenate(
            [
                lax.ppermute(tail, axis, [(i, (i + 1) % count) for i in range(ends)]),
                cells,
                lax.ppermute(head, axis, [((i + 1) % count, i) for i in range(ends)]),
            ],
            axis=dim,
        )
    return cells


def xor_sum(cells, axis):
    count = lax.axis_size(axis)
    step = 1
    while step < count:
        cells = cells + lax.ppermute(cells, axis, [(i, i ^ step) for i in range(count)])
        step *= 2
    return cells


def product(form, left, right):
    return jnp.einsum(form, left, right, preferred_element_type=jnp.float32)


def normalize(raw_field, norm_gain, head_count):
    floats = raw_field.astype(jnp.float32)
    floats = floats.reshape(floats.shape[:-1] + (head_count, norm_gain.shape[0]))
    inverse = lax.rsqrt(jnp.mean(floats * floats, axis=-1, keepdims=True) + NORM_EPS)
    normed = floats * inverse
    return (normed, inverse, (normed * norm_gain).astype(jnp.bfloat16))


def norm_backward(upstream, normed, inverse, norm_gain):
    gain_part = jnp.sum(upstream * normed, axis=tuple(range(upstream.ndim - 1)))
    scaled = upstream * norm_gain
    raw_grad = inverse * (scaled - normed * jnp.mean(scaled * normed, axis=-1, keepdims=True))
    return (raw_grad, gain_part)


def open_pairs(windows, tile_size):
    span = 3 * tile_size
    spots = jnp.arange(span * span, dtype=jnp.int32)
    step_rows = spots // span // tile_size - 1
    step_cols = spots % span // tile_size - 1
    tile_row = lax.axis_index("ty") + step_rows
    tile_col = lax.axis_index("tx") + step_cols
    inside = (
        (tile_row >= 0)
        & (tile_row < lax.axis_size("ty"))
        & (tile_col >= 0)
        & (tile_col < lax.axis_size("tx"))
    )
    reach_rows = ((windows[:, 0] - 1) // 2)[:, None]
    reach_cols = ((windows[:, 1] - 1) // 2)[:, None]
    within = (jnp.abs(step_rows)[None, :] <= reach_rows) & (
        jnp.abs(step_cols)[None, :] <= reach_cols
    )
    return inside[None, :] & within


def gathered(cells, sides, width):
    for axis, dim in reversed(sides):
        count = lax.axis_size(axis)
        ends = count - 1
        full = cells.shape[dim]
        head = lax.slice_in_dim(cells, 0, width, axis=dim)
        middle = lax.slice_in_dim(cells, width, full - width, axis=dim).astype(jnp.float32)
        tail = lax.slice_in_dim(cells, full - width, full, axis=dim)
        from_right = lax.ppermute(head.astype(jnp.bfloat16), axis, [((i + 1) % count, i) for i in range(ends)])
        from_left = lax.ppermute(tail.astype(jnp.bfloat16), axis, [(i, (i + 1) % count) for i in range(ends)])
        cells = middle + from_right.astype(jnp.float32) + from_left.astype(jnp.float32)
    return cells


def raw_backward(upstream, normed, inverse, norm_gain):
    scaled = upstream * norm_gain
    return inverse * (scaled - normed * jnp.mean(scaled * normed, axis=-1, keepdims=True))


def query_side(queries, keys_near, values_near, grad_out, open_mask, score_scale):
    scores = product("qhc,mhc->hqm", queries, keys_near) * score_scale
    weights = jnp.where(open_mask[:, None, :], jnp.exp(scores), 0.0)
    totals = jnp.sum(weights, axis=2)
    shares = weights / totals[:, :, None]
    shares_low = shares.astype(jnp.bfloat16)
    output = product("hqm,mhc->qhc", shares_low, values_near).astype(jnp.bfloat16)
    output_back = lax.optimization_barrier(output).astype(jnp.float32)
    row_delta = jnp.sum(grad_out.astype(jnp.float32) * output_back, axis=-1)
    share_grad = product("qhc,mhc->hqm", grad_out, values_near)
    score_grad = (shares * (share_grad - row_delta.T[:, :, None])).astype(jnp.bfloat16)
    query_grad = product("hqm,mhc->qhc", score_grad, keys_near) * score_scale
    value_part = product("hqm,qhc->hmc", shares_low, grad_out)
    key_part = product("hqm,qhc->hmc", score_grad, queries) * score_scale
    return (output, query_grad, key_part, value_part)


def body(q_raw, k_raw, values, d_out, q_gain, k_gain, windows):
    head_count = windows.shape[0]
    share_len = q_gain.shape[0]
    head_size = share_len * lax.axis_size("fsdp")
    gain_slots = jnp.zeros((2, head_size), jnp.float32)
    gain_slots = lax.dynamic_update_slice_in_dim(
        gain_slots, jnp.stack([q_gain, k_gain]), lax.axis_index("fsdp") * share_len, 1
    )
    gains = xor_sum(gain_slots, "fsdp")
    q_gain_all, k_gain_all = gains[0], gains[1]
    frame_count, row_count, col_count, feature_count = q_raw.shape
    score_scale = 1.0 / math.sqrt(head_size)
    sides = (("tx", 3), ("ty", 2))
    arrived = padded(jnp.stack([k_raw, values]), sides, TILE)
    q_normed, q_inverse, q_hat = normalize(q_raw, q_gain_all, head_count)
    k_normed, k_inverse, _ = normalize(k_raw, k_gain_all, head_count)
    k_normed_near, _, k_hat_near = normalize(arrived[0], k_gain_all, head_count)
    open_mask = open_pairs(windows, TILE)
    local_rows = row_count * col_count
    near_rows = (row_count + 2 * TILE) * (col_count + 2 * TILE)

    def as_local(field):
        return field.reshape(frame_count, local_rows, head_count, head_size)

    def as_near(field):
        return field.reshape(frame_count, near_rows, head_count, head_size)

    def frame_query(queries, keys_near, values_near, grad_out):
        return query_side(queries, keys_near, values_near, grad_out, open_mask, score_scale)

    output, query_grad, key_part, value_part = jax.vmap(frame_query)(
        as_local(q_hat), as_near(k_hat_near), as_near(arrived[1]), as_local(d_out)
    )
    q_upstream = query_grad.reshape(q_normed.shape)
    q_part = jnp.sum(q_upstream * q_normed, axis=(0, 1, 2, 3))
    k_part = jnp.sum(key_part * jnp.swapaxes(as_near(k_normed_near), 1, 2), axis=(0, 1, 2))
    gain_parts = jnp.stack([q_part, k_part])
    plane_sum = xor_sum(xor_sum(gain_parts, "tx"), "ty")
    plane_sum, key_part, value_part = lax.optimization_barrier((plane_sum, key_part, value_part))
    owner_count = lax.axis_size("fsdp")
    pieces = plane_sum.reshape(2, owner_count, share_len).transpose(1, 0, 2)
    owned = lax.all_to_all(pieces, "fsdp", 0, 0, tiled=True).sum(axis=0)
    near_shape = (frame_count, head_count, row_count + 2 * TILE, col_count + 2 * TILE, head_size)

    def summed_of(part):
        cells = gathered(part.reshape(near_shape), sides, TILE)
        return cells.transpose(0, 2, 3, 1, 4)

    key_summed = summed_of(key_part)
    value_summed = summed_of(value_part)
    k_upstream = key_summed.reshape(k_normed.shape)
    q_field_grad = raw_backward(q_upstream, q_normed, q_inverse, q_gain_all)
    k_field_grad = raw_backward(k_upstream, k_normed, k_inverse, k_gain_all)
    return (
        output.reshape(q_raw.shape),
        q_field_grad.reshape(q_raw.shape).astype(jnp.bfloat16),
        k_field_grad.reshape(k_raw.shape).astype(jnp.bfloat16),
        value_summed.reshape(values.shape).astype(jnp.bfloat16),
        owned[0],
        owned[1],
    )


def solution(mesh):
    return jax.shard_map(
        body,
        mesh=mesh,
        in_specs=(
            P("fsdp", "ty", "tx", None),
            P("fsdp", "ty", "tx", None),
            P("fsdp", "ty", "tx", None),
            P("fsdp", "ty", "tx", None),
            P("fsdp"),
            P("fsdp"),
            P(),
        ),
        out_specs=(
            P("fsdp", "ty", "tx", None),
            P("fsdp", "ty", "tx", None),
            P("fsdp", "ty", "tx", None),
            P("fsdp", "ty", "tx", None),
            P("fsdp"),
            P("fsdp"),
        ),
        check_vma=False,
    )
```

```python
import math

import jax
import jax.numpy as jnp
from jax import lax
from jax.sharding import PartitionSpec as P

TILE = 8


NORM_EPS = 1e-06


def padded(cells, sides, width):
    for axis, dim in sides:
        count = lax.axis_size(axis)
        ends = count - 1
        head = lax.slice_in_dim(cells, 0, width, axis=dim)
        tail = lax.slice_in_dim(cells, cells.shape[dim] - width, cells.shape[dim], axis=dim)
        cells = jnp.concatenate(
            [
                lax.ppermute(tail, axis, [(i, (i + 1) % count) for i in range(ends)]),
                cells,
                lax.ppermute(head, axis, [((i + 1) % count, i) for i in range(ends)]),
            ],
            axis=dim,
        )
    return cells


def xor_sum(cells, axis):
    count = lax.axis_size(axis)
    step = 1
    while step < count:
        cells = cells + lax.ppermute(cells, axis, [(i, i ^ step) for i in range(count)])
        step *= 2
    return cells


def product(form, left, right):
    return jnp.einsum(form, left, right, preferred_element_type=jnp.float32)


def normalize(raw_field, norm_gain, head_count):
    floats = raw_field.astype(jnp.float32)
    floats = floats.reshape(floats.shape[:-1] + (head_count, norm_gain.shape[0]))
    inverse = lax.rsqrt(jnp.mean(floats * floats, axis=-1, keepdims=True) + NORM_EPS)
    normed = floats * inverse
    return (normed, inverse, (normed * norm_gain).astype(jnp.bfloat16))


def norm_backward(upstream, normed, inverse, norm_gain):
    gain_part = jnp.sum(upstream * normed, axis=tuple(range(upstream.ndim - 1)))
    scaled = upstream * norm_gain
    raw_grad = inverse * (scaled - normed * jnp.mean(scaled * normed, axis=-1, keepdims=True))
    return (raw_grad, gain_part)


def open_pairs(windows, tile_size):
    span = 3 * tile_size
    spots = jnp.arange(span * span, dtype=jnp.int32)
    step_rows = spots // span // tile_size - 1
    step_cols = spots % span // tile_size - 1
    tile_row = lax.axis_index("ty") + step_rows
    tile_col = lax.axis_index("tx") + step_cols
    inside = (
        (tile_row >= 0)
        & (tile_row < lax.axis_size("ty"))
        & (tile_col >= 0)
        & (tile_col < lax.axis_size("tx"))
    )
    reach_rows = ((windows[:, 0] - 1) // 2)[:, None]
    reach_cols = ((windows[:, 1] - 1) // 2)[:, None]
    within = (jnp.abs(step_rows)[None, :] <= reach_rows) & (
        jnp.abs(step_cols)[None, :] <= reach_cols
    )
    return inside[None, :] & within


def gathered(cells, sides, width):
    for axis, dim in reversed(sides):
        count = lax.axis_size(axis)
        ends = count - 1
        full = cells.shape[dim]
        head = lax.slice_in_dim(cells, 0, width, axis=dim)
        middle = lax.slice_in_dim(cells, width, full - width, axis=dim).astype(jnp.float32)
        tail = lax.slice_in_dim(cells, full - width, full, axis=dim)
        from_right = lax.ppermute(head.astype(jnp.bfloat16), axis, [((i + 1) % count, i) for i in range(ends)])
        from_left = lax.ppermute(tail.astype(jnp.bfloat16), axis, [(i, (i + 1) % count) for i in range(ends)])
        cells = middle + from_right.astype(jnp.float32) + from_left.astype(jnp.float32)
    return cells


def raw_backward(upstream, normed, inverse, norm_gain):
    scaled = upstream * norm_gain
    return inverse * (scaled - normed * jnp.mean(scaled * normed, axis=-1, keepdims=True))


def query_side(queries, keys_near, values_near, grad_out, open_mask, score_scale):
    scores = product("qhc,mhc->hqm", queries, keys_near) * score_scale
    weights = jnp.where(open_mask[:, None, :], jnp.exp(scores), 0.0)
    totals = jnp.sum(weights, axis=2)
    shares = weights / totals[:, :, None]
    shares_low = shares.astype(jnp.bfloat16)
    output = product("hqm,mhc->qhc", shares_low, values_near).astype(jnp.bfloat16)
    output_back = lax.optimization_barrier(output).astype(jnp.float32)
    row_delta = jnp.sum(grad_out.astype(jnp.float32) * output_back, axis=-1)
    share_grad = product("qhc,mhc->hqm", grad_out, values_near)
    score_grad = (shares * (share_grad - row_delta.T[:, :, None])).astype(jnp.bfloat16)
    query_grad = product("hqm,mhc->qhc", score_grad, keys_near) * score_scale
    value_part = product("hqm,qhc->hmc", shares_low, grad_out)
    key_part = product("hqm,qhc->hmc", score_grad, queries) * score_scale
    return (output, query_grad, key_part, value_part)


def body(q_raw, k_raw, values, d_out, q_gain, k_gain, windows):
    head_count = windows.shape[0]
    share_len = q_gain.shape[0]
    head_size = share_len * lax.axis_size("fsdp")
    owner_count = lax.axis_size("fsdp")
    own_gains = jnp.broadcast_to(jnp.stack([q_gain, k_gain])[None], (owner_count, 2, share_len))
    gathered_gains = lax.all_to_all(own_gains, "fsdp", 0, 0, tiled=True)
    gains = gathered_gains.transpose(1, 0, 2).reshape(2, head_size)
    q_gain_all, k_gain_all = gains[0], gains[1]
    frame_count, row_count, col_count, feature_count = q_raw.shape
    score_scale = 1.0 / math.sqrt(head_size)
    sides = (("tx", 3), ("ty", 2))
    arrived = padded(jnp.stack([k_raw, values]), sides, TILE)
    q_normed, q_inverse, q_hat = normalize(q_raw, q_gain_all, head_count)
    k_normed, k_inverse, _ = normalize(k_raw, k_gain_all, head_count)
    k_normed_near, _, k_hat_near = normalize(arrived[0], k_gain_all, head_count)
    open_mask = open_pairs(windows, TILE)
    local_rows = row_count * col_count
    near_rows = (row_count + 2 * TILE) * (col_count + 2 * TILE)

    def as_local(field):
        return field.reshape(frame_count, local_rows, head_count, head_size)

    def as_near(field):
        return field.reshape(frame_count, near_rows, head_count, head_size)

    def frame_query(queries, keys_near, values_near, grad_out):
        return query_side(queries, keys_near, values_near, grad_out, open_mask, score_scale)

    output, query_grad, key_part, value_part = jax.vmap(frame_query)(
        as_local(q_hat), as_near(k_hat_near), as_near(arrived[1]), as_local(d_out)
    )
    q_upstream = query_grad.reshape(q_normed.shape)
    q_part = jnp.sum(q_upstream * q_normed, axis=(0, 1, 2, 3))
    k_part = jnp.sum(key_part * jnp.swapaxes(as_near(k_normed_near), 1, 2), axis=(0, 1, 2))
    gain_parts = jnp.stack([q_part, k_part])
    plane_sum = xor_sum(xor_sum(gain_parts, "tx"), "ty")
    plane_sum, key_part, value_part = lax.optimization_barrier((plane_sum, key_part, value_part))
    owner_count = lax.axis_size("fsdp")
    pieces = plane_sum.reshape(2, owner_count, share_len).transpose(1, 0, 2)
    owned = lax.all_to_all(pieces, "fsdp", 0, 0, tiled=True).sum(axis=0)
    near_shape = (frame_count, head_count, row_count + 2 * TILE, col_count + 2 * TILE, head_size)

    def summed_of(part):
        cells = gathered(part.reshape(near_shape), sides, TILE)
        return cells.transpose(0, 2, 3, 1, 4)

    key_summed = summed_of(key_part)
    value_summed = summed_of(value_part)
    k_upstream = key_summed.reshape(k_normed.shape)
    q_field_grad = raw_backward(q_upstream, q_normed, q_inverse, q_gain_all)
    k_field_grad = raw_backward(k_upstream, k_normed, k_inverse, k_gain_all)
    return (
        output.reshape(q_raw.shape),
        q_field_grad.reshape(q_raw.shape).astype(jnp.bfloat16),
        k_field_grad.reshape(k_raw.shape).astype(jnp.bfloat16),
        value_summed.reshape(values.shape).astype(jnp.bfloat16),
        owned[0],
        owned[1],
    )


def solution(mesh):
    return jax.shard_map(
        body,
        mesh=mesh,
        in_specs=(
            P("fsdp", "ty", "tx", None),
            P("fsdp", "ty", "tx", None),
            P("fsdp", "ty", "tx", None),
            P("fsdp", "ty", "tx", None),
            P("fsdp"),
            P("fsdp"),
            P(),
        ),
        out_specs=(
            P("fsdp", "ty", "tx", None),
            P("fsdp", "ty", "tx", None),
            P("fsdp", "ty", "tx", None),
            P("fsdp", "ty", "tx", None),
            P("fsdp"),
            P("fsdp"),
        ),
        check_vma=False,
    )
```

```python
import math

import jax
import jax.numpy as jnp
from jax import lax
from jax.sharding import PartitionSpec as P


TILE = 8


NORM_EPS = 1e-06


def padded(cells, sides, width):
    for axis, dim in sides:
        count = lax.axis_size(axis)
        ends = count - 1
        head = lax.slice_in_dim(cells, 0, width, axis=dim)
        tail = lax.slice_in_dim(cells, cells.shape[dim] - width, cells.shape[dim], axis=dim)
        cells = jnp.concatenate(
            [
                lax.ppermute(tail, axis, [(i, (i + 1) % count) for i in range(ends)]),
                cells,
                lax.ppermute(head, axis, [((i + 1) % count, i) for i in range(ends)]),
            ],
            axis=dim,
        )
    return cells


def xor_sum(cells, axis):
    count = lax.axis_size(axis)
    step = 1
    while step < count:
        cells = cells + lax.ppermute(cells, axis, [(i, i ^ step) for i in range(count)])
        step *= 2
    return cells


def product(form, left, right):
    return jnp.einsum(form, left, right, preferred_element_type=jnp.float32)


def normalize(raw_field, norm_gain, head_count):
    floats = raw_field.astype(jnp.float32)
    floats = floats.reshape(floats.shape[:-1] + (head_count, norm_gain.shape[0]))
    inverse = lax.rsqrt(jnp.mean(floats * floats, axis=-1, keepdims=True) + NORM_EPS)
    normed = floats * inverse
    return (normed, inverse, (normed * norm_gain).astype(jnp.bfloat16))


def open_pairs(windows, tile_size):
    span = 3 * tile_size
    spots = jnp.arange(span * span, dtype=jnp.int32)
    step_rows = spots // span // tile_size - 1
    step_cols = spots % span // tile_size - 1
    tile_row = lax.axis_index("ty") + step_rows
    tile_col = lax.axis_index("tx") + step_cols
    inside = (
        (tile_row >= 0)
        & (tile_row < lax.axis_size("ty"))
        & (tile_col >= 0)
        & (tile_col < lax.axis_size("tx"))
    )
    reach_rows = ((windows[:, 0] - 1) // 2)[:, None]
    reach_cols = ((windows[:, 1] - 1) // 2)[:, None]
    within = (jnp.abs(step_rows)[None, :] <= reach_rows) & (
        jnp.abs(step_cols)[None, :] <= reach_cols
    )
    return inside[None, :] & within


def gathered(cells, sides, width):
    for axis, dim in reversed(sides):
        count = lax.axis_size(axis)
        ends = count - 1
        full = cells.shape[dim]
        head = lax.slice_in_dim(cells, 0, width, axis=dim)
        middle = lax.slice_in_dim(cells, width, full - width, axis=dim).astype(jnp.float32)
        tail = lax.slice_in_dim(cells, full - width, full, axis=dim)
        from_right = lax.ppermute(head.astype(jnp.bfloat16), axis, [((i + 1) % count, i) for i in range(ends)])
        from_left = lax.ppermute(tail.astype(jnp.bfloat16), axis, [(i, (i + 1) % count) for i in range(ends)])
        cells = middle + from_right.astype(jnp.float32) + from_left.astype(jnp.float32)
    return cells


def raw_backward(upstream, normed, inverse, norm_gain):
    scaled = upstream * norm_gain
    return inverse * (scaled - normed * jnp.mean(scaled * normed, axis=-1, keepdims=True))


def query_side(queries, keys_near, values_near, grad_out, open_mask, score_scale):
    scores = product("qhc,mhc->hqm", queries, keys_near) * score_scale
    weights = jnp.where(open_mask[:, None, :], jnp.exp(scores), 0.0)
    totals = jnp.sum(weights, axis=2)
    shares = weights / totals[:, :, None]
    shares_low = shares.astype(jnp.bfloat16)
    output = product("hqm,mhc->qhc", shares_low, values_near).astype(jnp.bfloat16)
    output_back = lax.optimization_barrier(output).astype(jnp.float32)
    row_delta = jnp.sum(grad_out.astype(jnp.float32) * output_back, axis=-1)
    share_grad = product("qhc,mhc->hqm", grad_out, values_near)
    score_grad = (shares * (share_grad - row_delta.T[:, :, None])).astype(jnp.bfloat16)
    query_grad = product("hqm,mhc->qhc", score_grad, keys_near) * score_scale
    value_part = product("hqm,qhc->hmc", shares_low, grad_out)
    key_part = product("hqm,qhc->hmc", score_grad, queries) * score_scale
    return (output, query_grad, key_part, value_part)


def body_steps(q_raw, k_raw, values, d_out, q_gain, k_gain, windows):
    head_count = windows.shape[0]
    share_len = q_gain.shape[0]
    head_size = share_len * lax.axis_size("fsdp")
    owner_count = lax.axis_size("fsdp")
    own_gains = jnp.broadcast_to(jnp.stack([q_gain, k_gain])[None], (owner_count, 2, share_len))
    gathered_gains = lax.all_to_all(own_gains, "fsdp", 0, 0, tiled=True)
    gains = gathered_gains.transpose(1, 0, 2).reshape(2, head_size)
    q_gain_all, k_gain_all = gains[0], gains[1]
    frame_count, row_count, col_count, _ = q_raw.shape
    score_scale = 1.0 / math.sqrt(head_size)
    sides = (("tx", 3), ("ty", 2))
    arrived = padded(jnp.stack([k_raw, values]), sides, TILE)
    q_normed, q_inverse, q_hat = normalize(q_raw, q_gain_all, head_count)
    k_normed, k_inverse, _ = normalize(k_raw, k_gain_all, head_count)
    k_normed_near, _, k_hat_near = normalize(arrived[0], k_gain_all, head_count)
    open_mask = open_pairs(windows, TILE)
    local_rows = row_count * col_count
    near_rows = (row_count + 2 * TILE) * (col_count + 2 * TILE)

    def as_local(field):
        return field.reshape(frame_count, local_rows, head_count, head_size)

    def as_near(field):
        return field.reshape(frame_count, near_rows, head_count, head_size)

    def frame_query(queries, keys_near, values_near, grad_out):
        return query_side(queries, keys_near, values_near, grad_out, open_mask, score_scale)

    output, query_grad, key_part, value_part = jax.vmap(frame_query)(
        as_local(q_hat), as_near(k_hat_near), as_near(arrived[1]), as_local(d_out)
    )
    q_upstream = query_grad.reshape(q_normed.shape)
    q_part = jnp.sum(q_upstream * q_normed, axis=(0, 1, 2, 3))
    k_part = jnp.sum(key_part * jnp.swapaxes(as_near(k_normed_near), 1, 2), axis=(0, 1, 2))
    gain_parts = jnp.stack([q_part, k_part])
    plane_sum = xor_sum(xor_sum(gain_parts, "tx"), "ty")
    plane_sum, key_part, value_part = lax.optimization_barrier((plane_sum, key_part, value_part))
    owner_count = lax.axis_size("fsdp")
    pieces = plane_sum.reshape(2, owner_count, share_len).transpose(1, 0, 2)
    owned = lax.all_to_all(pieces, "fsdp", 0, 0, tiled=True).sum(axis=0)
    near_shape = (frame_count, head_count, row_count + 2 * TILE, col_count + 2 * TILE, head_size)

    def summed_of(part):
        cells = gathered(part.reshape(near_shape), sides, TILE)
        return cells.transpose(0, 2, 3, 1, 4)

    key_summed = summed_of(key_part)
    value_summed = summed_of(value_part)
    k_upstream = key_summed.reshape(k_normed.shape)
    q_field_grad = raw_backward(q_upstream, q_normed, q_inverse, q_gain_all)
    k_field_grad = raw_backward(k_upstream, k_normed, k_inverse, k_gain_all)
    return (
        output.reshape(q_raw.shape),
        q_field_grad.reshape(q_raw.shape).astype(jnp.bfloat16),
        k_field_grad.reshape(k_raw.shape).astype(jnp.bfloat16),
        value_summed.reshape(values.shape).astype(jnp.bfloat16),
        owned[0],
        owned[1],
    )


def solution(mesh):
    return shard_mapped(mesh)


def shard_mapped(mesh):
    return jax.shard_map(
        body_steps,
        mesh=mesh,
        in_specs=(
            P("fsdp", "ty", "tx", None),
            P("fsdp", "ty", "tx", None),
            P("fsdp", "ty", "tx", None),
            P("fsdp", "ty", "tx", None),
            P("fsdp"),
            P("fsdp"),
            P(),
        ),
        out_specs=(
            P("fsdp", "ty", "tx", None),
            P("fsdp", "ty", "tx", None),
            P("fsdp", "ty", "tx", None),
            P("fsdp", "ty", "tx", None),
            P("fsdp"),
            P("fsdp"),
        ),
        check_vma=False,
    )
```

```python
import math

import jax
import jax.numpy as jnp
from jax import lax
from jax.sharding import PartitionSpec as P

TILE = 8


NORM_EPS = 1e-06


def padded(cells, sides, width):
    for axis, dim in sides:
        count = lax.axis_size(axis)
        ends = count - 1
        head = lax.slice_in_dim(cells, 0, width, axis=dim)
        tail = lax.slice_in_dim(cells, cells.shape[dim] - width, cells.shape[dim], axis=dim)
        cells = jnp.concatenate(
            [
                lax.ppermute(tail, axis, [(i, (i + 1) % count) for i in range(ends)]),
                cells,
                lax.ppermute(head, axis, [((i + 1) % count, i) for i in range(ends)]),
            ],
            axis=dim,
        )
    return cells


def xor_sum(cells, axis):
    count = lax.axis_size(axis)
    step = 1
    while step < count:
        cells = cells + lax.ppermute(cells, axis, [(i, i ^ step) for i in range(count)])
        step *= 2
    return cells


def product(form, left, right):
    return jnp.einsum(form, left, right, preferred_element_type=jnp.float32)


def normalize(raw_field, norm_gain, head_count):
    floats = raw_field.astype(jnp.float32)
    floats = floats.reshape(floats.shape[:-1] + (head_count, norm_gain.shape[0]))
    inverse = lax.rsqrt(jnp.mean(floats * floats, axis=-1, keepdims=True) + NORM_EPS)
    normed = floats * inverse
    return (normed, inverse, (normed * norm_gain).astype(jnp.bfloat16))


def norm_backward(upstream, normed, inverse, norm_gain):
    gain_part = jnp.sum(upstream * normed, axis=tuple(range(upstream.ndim - 1)))
    scaled = upstream * norm_gain
    raw_grad = inverse * (scaled - normed * jnp.mean(scaled * normed, axis=-1, keepdims=True))
    return (raw_grad, gain_part)


def open_pairs(windows, tile_size):
    span = 3 * tile_size
    spots = jnp.arange(span * span, dtype=jnp.int32)
    step_rows = spots // span // tile_size - 1
    step_cols = spots % span // tile_size - 1
    tile_row = lax.axis_index("ty") + step_rows
    tile_col = lax.axis_index("tx") + step_cols
    inside = (
        (tile_row >= 0)
        & (tile_row < lax.axis_size("ty"))
        & (tile_col >= 0)
        & (tile_col < lax.axis_size("tx"))
    )
    reach_rows = ((windows[:, 0] - 1) // 2)[:, None]
    reach_cols = ((windows[:, 1] - 1) // 2)[:, None]
    within = (jnp.abs(step_rows)[None, :] <= reach_rows) & (
        jnp.abs(step_cols)[None, :] <= reach_cols
    )
    return inside[None, :] & within


def gathered(cells, sides, width):
    for axis, dim in reversed(sides):
        count = lax.axis_size(axis)
        ends = count - 1
        full = cells.shape[dim]
        head = lax.slice_in_dim(cells, 0, width, axis=dim)
        middle = lax.slice_in_dim(cells, width, full - width, axis=dim).astype(jnp.float32)
        tail = lax.slice_in_dim(cells, full - width, full, axis=dim)
        from_right = lax.ppermute(head.astype(jnp.bfloat16), axis, [((i + 1) % count, i) for i in range(ends)])
        from_left = lax.ppermute(tail.astype(jnp.bfloat16), axis, [(i, (i + 1) % count) for i in range(ends)])
        cells = middle + from_right.astype(jnp.float32) + from_left.astype(jnp.float32)
    return cells


def raw_backward(upstream, normed, inverse, norm_gain):
    scaled = upstream * norm_gain
    return inverse * (scaled - normed * jnp.mean(scaled * normed, axis=-1, keepdims=True))


def query_side(queries, keys_near, values_near, grad_out, open_mask, score_scale):
    scores = product("qhc,mhc->hqm", queries, keys_near) * score_scale
    weights = jnp.where(open_mask[:, None, :], jnp.exp(scores), 0.0)
    totals = jnp.sum(weights, axis=2)
    shares = weights / totals[:, :, None]
    shares_low = shares.astype(jnp.bfloat16)
    output = product("hqm,mhc->qhc", shares_low, values_near).astype(jnp.bfloat16)
    output_back = lax.optimization_barrier(output).astype(jnp.float32)
    row_delta = jnp.sum(grad_out.astype(jnp.float32) * output_back, axis=-1)
    share_grad = product("qhc,mhc->hqm", grad_out, values_near)
    score_grad = (shares * (share_grad - row_delta.T[:, :, None])).astype(jnp.bfloat16)
    query_grad = product("hqm,mhc->qhc", score_grad, keys_near) * score_scale
    value_part = product("hqm,qhc->hmc", shares_low, grad_out)
    key_part = product("hqm,qhc->hmc", score_grad, queries) * score_scale
    return (output, query_grad, key_part, value_part)


def body(q_raw, k_raw, values, d_out, q_gain, k_gain, windows):
    head_count = windows.shape[0]
    share_len = q_gain.shape[0]
    head_size = share_len * lax.axis_size("fsdp")
    owner_count = lax.axis_size("fsdp")
    own_gains = jnp.broadcast_to(jnp.stack([q_gain, k_gain])[None], (owner_count, 2, share_len))
    gathered_gains = lax.all_to_all(own_gains, "fsdp", 0, 0, tiled=True)
    gains = gathered_gains.transpose(1, 0, 2).reshape(2, head_size)
    q_gain_all, k_gain_all = gains[0], gains[1]
    frame_count, row_count, col_count, feature_count = q_raw.shape
    score_scale = 1.0 / math.sqrt(head_size)
    sides = (("tx", 3), ("ty", 2))
    arrived = padded(jnp.stack([k_raw, values]), sides, TILE)
    q_normed, q_inverse, q_hat = normalize(q_raw, q_gain_all, head_count)
    k_normed, k_inverse, _ = normalize(k_raw, k_gain_all, head_count)
    k_normed_near, _, k_hat_near = normalize(arrived[0], k_gain_all, head_count)
    open_mask = open_pairs(windows, TILE)
    local_rows = row_count * col_count
    near_rows = (row_count + 2 * TILE) * (col_count + 2 * TILE)

    def as_local(field):
        return field.reshape(frame_count, local_rows, head_count, head_size)

    def as_near(field):
        return field.reshape(frame_count, near_rows, head_count, head_size)

    def frame_query(queries, keys_near, values_near, grad_out):
        return query_side(queries, keys_near, values_near, grad_out, open_mask, score_scale)

    output, query_grad, key_part, value_part = jax.vmap(frame_query)(
        as_local(q_hat), as_near(k_hat_near), as_near(arrived[1]), as_local(d_out)
    )
    q_upstream = query_grad.reshape(q_normed.shape)
    q_part = jnp.sum(q_upstream * q_normed, axis=(0, 1, 2, 3))
    k_part = jnp.sum(key_part * jnp.swapaxes(as_near(k_normed_near), 1, 2), axis=(0, 1, 2))
    gain_parts = jnp.stack([q_part, k_part])
    plane_sum = xor_sum(xor_sum(gain_parts, "tx"), "ty")
    owner_count = lax.axis_size("fsdp")
    pieces = plane_sum.reshape(2, owner_count, share_len).transpose(1, 0, 2)
    owned = lax.all_to_all(pieces, "fsdp", 0, 0, tiled=True).sum(axis=0)
    near_shape = (frame_count, head_count, row_count + 2 * TILE, col_count + 2 * TILE, head_size)

    def summed_of(part):
        cells = gathered(part.reshape(near_shape), sides, TILE)
        return cells.transpose(0, 2, 3, 1, 4)

    key_summed = summed_of(key_part)
    value_summed = summed_of(value_part)
    k_upstream = key_summed.reshape(k_normed.shape)
    q_field_grad = raw_backward(q_upstream, q_normed, q_inverse, q_gain_all)
    k_field_grad = raw_backward(k_upstream, k_normed, k_inverse, k_gain_all)
    return (
        output.reshape(q_raw.shape),
        q_field_grad.reshape(q_raw.shape).astype(jnp.bfloat16),
        k_field_grad.reshape(k_raw.shape).astype(jnp.bfloat16),
        value_summed.reshape(values.shape).astype(jnp.bfloat16),
        owned[0],
        owned[1],
    )


def solution(mesh):
    return jax.shard_map(
        body,
        mesh=mesh,
        in_specs=(
            P("fsdp", "ty", "tx", None),
            P("fsdp", "ty", "tx", None),
            P("fsdp", "ty", "tx", None),
            P("fsdp", "ty", "tx", None),
            P("fsdp"),
            P("fsdp"),
            P(),
        ),
        out_specs=(
            P("fsdp", "ty", "tx", None),
            P("fsdp", "ty", "tx", None),
            P("fsdp", "ty", "tx", None),
            P("fsdp", "ty", "tx", None),
            P("fsdp"),
            P("fsdp"),
        ),
        check_vma=False,
    )
```
